128 devices in a mesh: expert: 16 (over z_hi, x, core), dp: 8 (over y, z_lo).
Axes of the slice: x: 4, y: 4, z: 4 (z_hi: 2, z_lo: 2; z = z_hi * 2 + z_lo), core: 2. Of those that a mesh axis runs over, the one named last changes fastest.
Arguments:
- tokens: bfloat16 [16384, 2048], P(('expert', 'dp')), may hold values from -6 to 6
- routes: int32 [16384, 2], P(('expert', 'dp')), may hold values from 0 to 127, all different within a row; in each aligned block of 128 rows (0 to 127, 128 to 255, ...) at most 4 rows name the same one
- gate_probs: float32 [16384, 2], P(('expert', 'dp')), may hold values from 0.05 to 1
- norm_gain: float32 [2048], replicated, may hold values from 0.1 to 1.9
- w_gate: bfloat16 [128, 2048, 768], P(('expert', 'dp')), may hold values from -0.125 to 0.125
- w_up: bfloat16 [128, 2048, 768], P(('expert', 'dp')), may hold values from -0.125 to 0.125
- w_down: bfloat16 [128, 768, 2048], P(('expert', 'dp')), may hold values from -0.21875 to 0.21875
- out_grad: bfloat16 [16384, 2048], P(('expert', 'dp')), may hold values from -6 to 6
Outputs:
- mixed: bfloat16 [16384, 2048], P(('expert', 'dp'))
- grad_probs: float32 [16384, 2], P(('expert', 'dp'))
- grad_gain: float32 [2048], replicated
- grad_tokens: bfloat16 [16384, 2048], P(('expert', 'dp'))
- grad_gate: bfloat16 [128, 2048, 768], P(('expert', 'dp'))
- grad_up: bfloat16 [128, 2048, 768], P(('expert', 'dp'))
- grad_down: bfloat16 [128, 768, 2048], P(('expert', 'dp'))
The draws below stay inside these ranges and needn't reach their ends.
Inputs may be any that keep to these rules, and one draw needn't show every extreme that they name: `routes`: each row names 2 different experts. Among the 128 rows of one device no expert is named more than 4 times, a bound that some block reaches.
All inputs are finite; a program needn't handle non-finite values.
Results may differ from the reference program's by a relative error of at most 0.0072.
Values may be sent and summed in bfloat16 or wider, within the bound.
No kernel may reach another device: no remote copies, remote signals or barrier semaphores. Data moves between devices by JAX's collectives and lax.ppermute only.
A program may use at most 128 MiB of HBM per device.

```python
import math
import jax
import jax.numpy as jnp
import numpy as np
from jax import lax

D = 2048
FF = 768
TOP = 2
TOK_DEV = 128
EXPERTS = 128
TOKENS = 16384
MOST = 4


def levels(own_key, extent, pieces, least, high):
    loudness, own = 1.0, jax.random.fold_in(own_key, 6)
    for position, blocks in pieces:
        draws = jnp.exp(jax.random.uniform(jax.random.fold_in(own, position), (blocks,), jnp.float32, least / len(pieces), high / len(pieces)))
        loudness = loudness * jnp.repeat(draws, extent[position] // blocks).reshape([-1 if axis == position else 1 for axis in range(len(extent))])
    return loudness


def routed_block(rng, own, number, rows, number_of, top, limit, skew):
    ranking = jax.random.permutation(rng, number_of)
    heavy_load, common = shares(number_of, rows * top, limit, skew, True), shares(number_of, rows * top, limit, skew, False)
    places = jnp.arange(number_of)

    def named(lengths, offset_by):
        used = int((lengths > 0).sum())
        fixed = max(1, used // 4)
        moved = fixed + (places - fixed + offset_by * (used - fixed)) % max(1, number_of - fixed)
        return jnp.zeros((number_of,), jnp.int32).at[ranking[jnp.where(places < fixed, places, moved)]].set(jnp.asarray(lengths, jnp.int32))

    lengths = jnp.where(number % 4 == 0, named(heavy_load, number // 4), named(common, number - number // 4 - 1))
    mixed = jax.random.permutation(jax.random.fold_in(own, 3), number_of)
    donor, sink = mixed[0:number_of // 2 * 2:2], mixed[1:number_of // 2 * 2:2]
    slack = jnp.minimum(lengths[donor] - 1, limit - lengths[sink]) // 2
    slack = jnp.where((donor == ranking[0]) | (sink == ranking[0]) | (lengths[sink] == 0), 0, jnp.maximum(slack, 0))
    moved = jax.random.randint(jax.random.fold_in(own, 4), (number_of // 2,), 0, 1 << 20) % (slack + 1)
    lengths = lengths.at[donor].add(-moved).at[sink].add(moved)
    items = jnp.searchsorted(jnp.cumsum(lengths), jnp.arange(rows * top), side="right").astype(jnp.int32)
    listing = items.reshape(top, rows).T
    listing = listing[jax.random.permutation(jax.random.fold_in(own, 1), rows)]
    offset_by = jax.random.randint(jax.random.fold_in(own, 2), (rows, 1), 0, top)
    return jnp.take_along_axis(listing, (jnp.arange(top)[None, :] + offset_by) % top, axis=1)


def shares(count, total, bound, slope, full):
    portions = [(1 << 20) // math.isqrt(grade ** slope) + 1 for grade in range(1, count + 1)]
    largest = bound if full else min(bound, max(-(-total // count), total * portions[0] // sum(portions)))
    least = 1 if total - largest >= count - 1 else 0
    holding, spare = [largest] + [least] * (count - 1), total - largest - least * (count - 1)
    while spare > 0:
        free = [i for i in range(1, count) if holding[i] < largest] or [i for i in range(1, count) if holding[i] < bound]
        whole, budget = sum([portions[i] for i in free]), spare
        for i in free:
            more = min(bound - holding[i], max(1, budget * portions[i] // whole), spare)
            holding[i] = holding[i] + more
            spare = spare - more
    return np.array(holding)


def scatter_about(rng, shape, scale, bound, split=(), kind=jnp.bfloat16):
    factor_of = levels(rng, shape, split, -0.22, 0.18) if split else 1.0
    drawn = jax.random.normal(rng, shape, jnp.float32) * scale * factor_of
    return jnp.minimum(jnp.maximum(drawn, -bound), bound).astype(kind)


def setup_inputs(seed: int = 0) -> dict:
    seeds = jax.random.split(jax.random.key(seed), 9)
    tokens = scatter_about(seeds[0], (TOKENS, D), 1.0, 6.0, ((0, 128),))
    routes_keys = jax.random.split(jax.random.fold_in(seeds[1], 1), TOKENS // TOK_DEV)
    routes_turns = jax.random.permutation(jax.random.fold_in(seeds[1], 3), TOKENS // TOK_DEV)
    routes = jax.vmap(lambda own, number: routed_block(jax.random.fold_in(seeds[1], 2), own, number, TOK_DEV, EXPERTS, TOP, MOST, 4))(routes_keys, routes_turns).reshape((TOKENS, TOP))
    gate_probs = jnp.clip(jnp.exp(math.log(1.0) - 2.9957323 * jax.random.uniform(seeds[2], (TOKENS, TOP), jnp.float32) ** levels(seeds[2], (TOKENS, TOP), ((0, 128),), -0.2, 0.2)), 0.05, 1.0)
    norm_gain = jnp.clip(1.0 + 0.18 * jax.random.normal(seeds[3], (D,), jnp.float32), 0.1, 1.9)
    w_gate = scatter_about(seeds[4], (EXPERTS, D, FF), D ** -0.5, 0.125, ((0, 128),))
    w_up = scatter_about(seeds[5], (EXPERTS, D, FF), D ** -0.5, 0.125, ((0, 128),))
    w_down = scatter_about(seeds[6], (EXPERTS, FF, D), FF ** -0.5, 0.21875, ((0, 128),))
    out_grad = scatter_about(seeds[7], (TOKENS, D), 1.0, 6.0, ((0, 128),))
    return dict(tokens=tokens, routes=routes, gate_probs=gate_probs, norm_gain=norm_gain, w_gate=w_gate, w_up=w_up, w_down=w_down, out_grad=out_grad)


def slots_of(block_ids):
    onehot = (block_ids[:, None] == jnp.arange(EXPERTS, dtype=jnp.int32)[None, :]).astype(jnp.int32)
    earlier = jnp.cumsum(onehot, axis=0) - onehot
    return (block_ids * MOST + lax.optimization_barrier(jnp.sum(earlier * onehot, axis=1))).astype(jnp.int32)

def expert_pass(packed):
    arrived, arrived_grad, gate_matrix, up_matrix, down_matrix = packed
    pre_gate = jnp.dot(arrived, gate_matrix, preferred_element_type=jnp.float32)
    up_value = jnp.dot(arrived, up_matrix, preferred_element_type=jnp.float32)
    sigmoid_gate = jax.nn.sigmoid(pre_gate)
    activated = pre_gate * sigmoid_gate
    hidden = (activated * up_value).astype(jnp.bfloat16)
    expert_out = jnp.dot(hidden, down_matrix, preferred_element_type=jnp.float32).astype(jnp.bfloat16)
    grad_hidden = lax.dot_general(arrived_grad, down_matrix, (((1,), (1,)), ((), ())), preferred_element_type=jnp.float32)
    grad_down = lax.dot_general(hidden, arrived_grad, (((0,), (0,)), ((), ())), preferred_element_type=jnp.float32).astype(jnp.bfloat16)
    grad_pre = (grad_hidden * up_value * sigmoid_gate * (1.0 + pre_gate * (1.0 - sigmoid_gate))).astype(jnp.bfloat16)
    grad_upval = (grad_hidden * activated).astype(jnp.bfloat16)
    grad_back = (lax.dot_general(grad_pre, gate_matrix, (((1,), (1,)), ((), ())), preferred_element_type=jnp.float32) + lax.dot_general(grad_upval, up_matrix, (((1,), (1,)), ((), ())), preferred_element_type=jnp.float32)).astype(jnp.bfloat16)
    grad_gate = lax.dot_general(arrived, grad_pre, (((0,), (0,)), ((), ())), preferred_element_type=jnp.float32).astype(jnp.bfloat16)
    grad_up = lax.dot_general(arrived, grad_upval, (((0,), (0,)), ((), ())), preferred_element_type=jnp.float32).astype(jnp.bfloat16)
    return (expert_out, grad_back, grad_gate, grad_up, grad_down)

def place(slot_index, rows):
    return jnp.zeros((EXPERTS * MOST, D), rows.dtype).at[slot_index].set(rows)

def to_experts(buffers, blocks):
    return buffers.reshape(blocks, EXPERTS, MOST, D).transpose(1, 0, 2, 3).reshape(EXPERTS, blocks * MOST, D)

def from_experts(buffers, blocks):
    return buffers.reshape(EXPERTS, blocks, MOST, D).transpose(1, 0, 2, 3).reshape(blocks, EXPERTS * MOST, D)

def pick(buffer, slot_index):
    return buffer[slot_index]

def reference(tokens, routes, gate_probs, norm_gain, w_gate, w_up, w_down, out_grad):
    blocks = TOKENS // TOK_DEV
    assigned = TOK_DEV * TOP
    inputs = tokens.astype(jnp.float32)
    inverse_rms = lax.rsqrt(lax.optimization_barrier(jnp.mean(inputs * inputs, axis=1, keepdims=True)) + 1e-06)
    normed = inputs * inverse_rms
    scaled = (normed * norm_gain).astype(jnp.bfloat16)
    slots = jax.vmap(slots_of)(routes.reshape(blocks, assigned).astype(jnp.int32))
    rows = jnp.repeat(scaled, TOP, axis=0).reshape(blocks, assigned, D)
    sent = to_experts(jax.vmap(place)(slots, rows), blocks)
    grad_in = out_grad.astype(jnp.float32)
    weights = gate_probs[:, :, None]
    grad_rows = (weights * grad_in[:, None, :]).astype(jnp.bfloat16).reshape(blocks, assigned, D)
    sent_grad = to_experts(jax.vmap(place)(slots, grad_rows), blocks)
    expert_out, grad_back, grad_gate, grad_up, grad_down = lax.map(expert_pass, (sent, sent_grad, w_gate, w_up, w_down))
    picked = jax.vmap(pick)(from_experts(expert_out, blocks), slots).reshape(TOKENS, TOP, D).astype(jnp.float32)
    mixed = (inputs + lax.optimization_barrier(jnp.sum(weights * picked, axis=1))).astype(jnp.bfloat16)
    grad_probs = lax.optimization_barrier(jnp.sum(grad_in[:, None, :] * picked, axis=2))
    back = jax.vmap(pick)(from_experts(grad_back, blocks), slots).reshape(TOKENS, TOP, D).astype(jnp.float32)
    grad_normed = lax.optimization_barrier(jnp.sum(back, axis=1))
    grad_gain = lax.optimization_barrier(jnp.sum(grad_normed * normed, axis=0))
    grad_scaled = grad_normed * norm_gain
    grad_tokens = (grad_in + inverse_rms * (grad_scaled - normed * lax.optimization_barrier(jnp.mean(grad_scaled * normed, axis=1, keepdims=True)))).astype(jnp.bfloat16)
    return (mixed, grad_probs, grad_gain, grad_tokens, grad_gate, grad_up, grad_down)
```

```python
import jax
import jax.numpy as jnp
from jax import lax
from jax.sharding import PartitionSpec as P

AXES = ("expert", "dp")


def exchange(rows):
    return lax.all_to_all(rows, AXES, split_axis=0, concat_axis=0, tiled=True)


def contract(left, right, left_dim, right_dim):
    return lax.dot_general(
        left, right, (((left_dim,), (right_dim,)), ((), ())), preferred_element_type=jnp.float32
    )


def all_sum(part, devices_all):
    total = part
    step = 1
    while step < devices_all:
        pairs = [(i, i ^ step) for i in range(devices_all)]
        total = total + lax.ppermute(total, AXES, pairs)
        step *= 2
    return total


def expert_pass(arrived, arrived_grad, gate_matrix, up_matrix, down_matrix):
    pre_gate = jnp.dot(arrived, gate_matrix, preferred_element_type=jnp.float32)
    up_value = jnp.dot(arrived, up_matrix, preferred_element_type=jnp.float32)
    sigmoid_gate = jax.nn.sigmoid(pre_gate)
    activated = pre_gate * sigmoid_gate
    hidden = (activated * up_value).astype(jnp.bfloat16)
    expert_out = jnp.dot(hidden, down_matrix, preferred_element_type=jnp.float32).astype(
        jnp.bfloat16
    )
    grad_hidden = contract(arrived_grad, down_matrix, 1, 1)
    grad_down = contract(hidden, arrived_grad, 0, 0).astype(jnp.bfloat16)
    grad_pre = (
        grad_hidden * up_value * sigmoid_gate * (1.0 + pre_gate * (1.0 - sigmoid_gate))
    ).astype(jnp.bfloat16)
    grad_upval = (grad_hidden * activated).astype(jnp.bfloat16)
    grad_back = (
        contract(grad_pre, gate_matrix, 1, 1) + contract(grad_upval, up_matrix, 1, 1)
    ).astype(jnp.bfloat16)
    grad_gate = contract(arrived, grad_pre, 0, 0).astype(jnp.bfloat16)
    grad_up = contract(arrived, grad_upval, 0, 0).astype(jnp.bfloat16)
    return expert_out, grad_back, grad_gate, grad_up, grad_down


def on_device(tokens, routes, gate_probs, norm_gain, w_gate, w_up, w_down, out_grad):
    devices_all = lax.axis_size(AXES)
    tok_rows, width = tokens.shape
    top_count = routes.shape[1]
    assigned = tok_rows * top_count
    capacity = 2 * assigned // devices_all
    slots = devices_all * capacity
    inputs = tokens.astype(jnp.float32)
    inverse_rms = lax.rsqrt(jnp.mean(inputs * inputs, axis=1, keepdims=True) + 1e-06)
    normed = inputs * inverse_rms
    scaled = (normed * norm_gain).astype(jnp.bfloat16)
    flat_ids = routes.reshape(assigned)
    onehot = (flat_ids[:, None] == jnp.arange(devices_all, dtype=jnp.int32)[None, :]).astype(
        jnp.int32
    )
    earlier = jnp.cumsum(onehot, axis=0) - onehot
    slot_index = flat_ids * capacity + jnp.sum(earlier * onehot, axis=1)
    select = (slot_index[:, None] == jnp.arange(slots, dtype=jnp.int32)[None, :]).astype(
        jnp.bfloat16
    )
    select_tk = select.reshape(tok_rows, top_count, slots)
    select_tok = jnp.sum(select_tk, axis=1)
    grad_in = out_grad.astype(jnp.float32)
    grad_rows = (gate_probs[:, :, None] * grad_in[:, None, :]).astype(jnp.bfloat16)
    send_scaled = contract(select_tok, scaled, 0, 0).astype(jnp.bfloat16)
    send_grad = lax.dot_general(
        select_tk, grad_rows, (((0, 1), (0, 1)), ((), ())), preferred_element_type=jnp.float32
    ).astype(jnp.bfloat16)
    sent = jnp.concatenate([send_scaled, send_grad], axis=1).reshape(
        devices_all, capacity, 2 * width
    )
    arrived_all = exchange(sent).reshape(slots, 2 * width)
    arrived = arrived_all[:, :width]
    arrived_grad = arrived_all[:, width:]
    expert_out, grad_back, grad_gate, grad_up, grad_down = expert_pass(
        arrived, arrived_grad, w_gate[0], w_up[0], w_down[0]
    )
    back = jnp.concatenate([expert_out, grad_back], axis=1).reshape(
        devices_all, capacity, 2 * width
    )
    returned = exchange(back).reshape(slots, 2 * width)
    picked = [
        contract(select_tk[:, k, :], returned, 1, 0) for k in range(top_count)
    ]
    outs = [p[:, :width] for p in picked]
    backs = [p[:, width:] for p in picked]
    combined = gate_probs[:, 0:1] * outs[0]
    for k in range(1, top_count):
        combined = combined + gate_probs[:, k : k + 1] * outs[k]
    mixed = (inputs + combined).astype(jnp.bfloat16)
    grad_probs = jnp.stack([jnp.sum(grad_in * o, axis=1) for o in outs], axis=1)
    grad_normed = backs[0]
    for k in range(1, top_count):
        grad_normed = grad_normed + backs[k]
    gain_part = jnp.sum(grad_normed * normed, axis=0)
    grad_gain = all_sum(gain_part, devices_all)
    grad_scaled = grad_normed * norm_gain
    grad_tokens = (
        grad_in
        + inverse_rms
        * (grad_scaled - normed * jnp.mean(grad_scaled * normed, axis=1, keepdims=True))
    ).astype(jnp.bfloat16)
    return (
        mixed,
        grad_probs,
        grad_gain,
        grad_tokens,
        grad_gate[None],
        grad_up[None],
        grad_down[None],
    )


def solution(mesh):
    rows = P(AXES, None)
    stacked = P(AXES, None, None)
    return jax.shard_map(
        on_device,
        mesh=mesh,
        in_specs=(rows, rows, rows, P(), stacked, stacked, stacked, rows),
        out_specs=(rows, rows, P(), rows, stacked, stacked, stacked),
        check_vma=False,
    )
```

```python
import jax
import jax.numpy as jnp
from jax import lax
from jax.sharding import PartitionSpec as P

AXES = ("expert", "dp")


def exchange(rows):
    return lax.all_to_all(rows, AXES, split_axis=0, concat_axis=0, tiled=True)


def contract(left, right, left_dim, right_dim):
    return lax.dot_general(
        left, right, (((left_dim,), (right_dim,)), ((), ())), preferred_element_type=jnp.float32
    )


def contract2(left, right):
    return lax.dot_general(
        left, right, (((0, 1), (0, 1)), ((), ())), preferred_element_type=jnp.float32
    )


def all_sum(part, devices_all):
    total = part
    step = 1
    while step < devices_all:
        pairs = [(i, i ^ step) for i in range(devices_all)]
        total = total + lax.ppermute(total, AXES, pairs)
        step *= 2
    return total


def expert_pass(arrived, arrived_grad, gate_matrix, up_matrix, down_matrix):
    pre_gate = contract(arrived, gate_matrix, 2, 0)
    up_value = contract(arrived, up_matrix, 2, 0)
    sigmoid_gate = jax.nn.sigmoid(pre_gate)
    activated = pre_gate * sigmoid_gate
    hidden = (activated * up_value).astype(jnp.bfloat16)
    expert_out = contract(hidden, down_matrix, 2, 0).astype(jnp.bfloat16)
    grad_hidden = contract(arrived_grad, down_matrix, 2, 1)
    grad_down = contract2(hidden, arrived_grad).astype(jnp.bfloat16)
    grad_pre = (
        grad_hidden * up_value * sigmoid_gate * (1.0 + pre_gate * (1.0 - sigmoid_gate))
    ).astype(jnp.bfloat16)
    grad_upval = (grad_hidden * activated).astype(jnp.bfloat16)
    grad_back = (
        contract(grad_pre, gate_matrix, 2, 1) + contract(grad_upval, up_matrix, 2, 1)
    ).astype(jnp.bfloat16)
    grad_gate = contract2(arrived, grad_pre).astype(jnp.bfloat16)
    grad_up = contract2(arrived, grad_upval).astype(jnp.bfloat16)
    return expert_out, grad_back, grad_gate, grad_up, grad_down


def on_device(tokens, routes, gate_probs, norm_gain, w_gate, w_up, w_down, out_grad):
    devices_all = lax.axis_size(AXES)
    tok_rows, width = tokens.shape
    top_count = routes.shape[1]
    assigned = tok_rows * top_count
    capacity = 2 * assigned // devices_all
    slots = devices_all * capacity
    inputs = tokens.astype(jnp.float32)
    inverse_rms = lax.rsqrt(jnp.mean(inputs * inputs, axis=1, keepdims=True) + 1e-06)
    normed = inputs * inverse_rms
    scaled = (normed * norm_gain).astype(jnp.bfloat16)
    flat_ids = routes.reshape(assigned)
    onehot = (flat_ids[:, None] == jnp.arange(devices_all, dtype=jnp.int32)[None, :]).astype(
        jnp.int32
    )
    earlier = jnp.cumsum(onehot, axis=0) - onehot
    slot_index = flat_ids * capacity + jnp.sum(earlier * onehot, axis=1)
    select = (slot_index[:, None] == jnp.arange(slots, dtype=jnp.int32)[None, :]).astype(
        jnp.bfloat16
    )
    select_tk = select.reshape(tok_rows, top_count, slots)
    select_tok = jnp.sum(select_tk, axis=1)
    grad_in = out_grad.astype(jnp.float32)
    grad_rows = (gate_probs[:, :, None] * grad_in[:, None, :]).astype(jnp.bfloat16)
    sel_tok3 = select_tok.reshape(tok_rows, devices_all, capacity)
    sel_tk3 = select_tk.reshape(tok_rows, top_count, devices_all, capacity)
    send_scaled = lax.dot_general(sel_tok3, scaled, (((0,), (0,)), ((), ())), preferred_element_type=jnp.float32).astype(jnp.bfloat16)
    send_grad = lax.dot_general(
        sel_tk3, grad_rows, (((0, 1), (0, 1)), ((), ())), preferred_element_type=jnp.float32
    ).astype(jnp.bfloat16)
    sent = jnp.concatenate([send_scaled, send_grad], axis=2)
    arrived_all = exchange(sent)
    arrived = arrived_all[:, :, :width]
    arrived_grad = arrived_all[:, :, width:]
    expert_out, grad_back, grad_gate, grad_up, grad_down = expert_pass(
        arrived, arrived_grad, w_gate[0], w_up[0], w_down[0]
    )
    back = jnp.concatenate([expert_out, grad_back], axis=2)
    returned = exchange(back)
    picked = [
        lax.dot_general(sel_tk3[:, k], returned, (((1, 2), (0, 1)), ((), ())), preferred_element_type=jnp.float32) for k in range(top_count)
    ]
    outs = [p[:, :width] for p in picked]
    backs = [p[:, width:] for p in picked]
    combined = gate_probs[:, 0:1] * outs[0]
    for k in range(1, top_count):
        combined = combined + gate_probs[:, k : k + 1] * outs[k]
    mixed = (inputs + combined).astype(jnp.bfloat16)
    grad_probs = jnp.stack([jnp.sum(grad_in * o, axis=1) for o in outs], axis=1)
    grad_normed = backs[0]
    for k in range(1, top_count):
        grad_normed = grad_normed + backs[k]
    gain_part = jnp.sum(grad_normed * normed, axis=0)
    grad_gain = all_sum(gain_part, devices_all)
    grad_scaled = grad_normed * norm_gain
    grad_tokens = (
        grad_in
        + inverse_rms
        * (grad_scaled - normed * jnp.mean(grad_scaled * normed, axis=1, keepdims=True))
    ).astype(jnp.bfloat16)
    return (
        mixed,
        grad_probs,
        grad_gain,
        grad_tokens,
        grad_gate[None],
        grad_up[None],
        grad_down[None],
    )


def solution(mesh):
    rows = P(AXES, None)
    stacked = P(AXES, None, None)
    return jax.shard_map(
        on_device,
        mesh=mesh,
        in_specs=(rows, rows, rows, P(), stacked, stacked, stacked, rows),
        out_specs=(rows, rows, P(), rows, stacked, stacked, stacked),
        check_vma=False,
    )
```

```python
import jax
import jax.numpy as jnp
from jax import lax
from jax.sharding import PartitionSpec as P

AXES = ("expert", "dp")


def exchange(rows):
    return lax.all_to_all(rows, AXES, split_axis=0, concat_axis=0, tiled=True)


def contract(left, right, left_dim, right_dim):
    return lax.dot_general(
        left, right, (((left_dim,), (right_dim,)), ((), ())), preferred_element_type=jnp.float32
    )


def all_sum(part, devices_all):
    me = lax.axis_index(AXES)
    total = part
    step = 1
    while step < devices_all:
        radix = 4 if step * 4 <= devices_all else 2
        held = [total] + [
            lax.ppermute(total, AXES, [(i, i ^ (x * step)) for i in range(devices_all)])
            for x in range(1, radix)
        ]
        position = (me // step) % radix
        canon = [lax.select_n(position ^ q, *held) for q in range(radix)]
        if radix == 4:
            total = (canon[0] + canon[1]) + (canon[2] + canon[3])
        else:
            total = canon[0] + canon[1]
        step *= radix
    return total


def expert_pass(arrived, arrived_grad, gate_matrix, up_matrix, down_matrix):
    pre_gate = jnp.dot(arrived, gate_matrix, preferred_element_type=jnp.float32)
    up_value = jnp.dot(arrived, up_matrix, preferred_element_type=jnp.float32)
    sigmoid_gate = jax.nn.sigmoid(pre_gate)
    activated = pre_gate * sigmoid_gate
    hidden = (activated * up_value).astype(jnp.bfloat16)
    expert_out = jnp.dot(hidden, down_matrix, preferred_element_type=jnp.float32).astype(
        jnp.bfloat16
    )
    grad_hidden = contract(arrived_grad, down_matrix, 1, 1)
    grad_down = contract(hidden, arrived_grad, 0, 0).astype(jnp.bfloat16)
    grad_pre = (
        grad_hidden * up_value * sigmoid_gate * (1.0 + pre_gate * (1.0 - sigmoid_gate))
    ).astype(jnp.bfloat16)
    grad_upval = (grad_hidden * activated).astype(jnp.bfloat16)
    grad_back = (
        contract(grad_pre, gate_matrix, 1, 1) + contract(grad_upval, up_matrix, 1, 1)
    ).astype(jnp.bfloat16)
    grad_gate = contract(arrived, grad_pre, 0, 0).astype(jnp.bfloat16)
    grad_up = contract(arrived, grad_upval, 0, 0).astype(jnp.bfloat16)
    return expert_out, grad_back, grad_gate, grad_up, grad_down


def on_device(tokens, routes, gate_probs, norm_gain, w_gate, w_up, w_down, out_grad):
    devices_all = lax.axis_size(AXES)
    tok_rows, width = tokens.shape
    top_count = routes.shape[1]
    assigned = tok_rows * top_count
    capacity = 2 * assigned // devices_all
    slots = devices_all * capacity
    inputs = tokens.astype(jnp.float32)
    inverse_rms = lax.rsqrt(jnp.mean(inputs * inputs, axis=1, keepdims=True) + 1e-06)
    normed = inputs * inverse_rms
    scaled = (normed * norm_gain).astype(jnp.bfloat16)
    flat_ids = routes.reshape(assigned)
    onehot = (flat_ids[:, None] == jnp.arange(devices_all, dtype=jnp.int32)[None, :]).astype(
        jnp.int32
    )
    earlier = jnp.cumsum(onehot, axis=0) - onehot
    slot_index = flat_ids * capacity + jnp.sum(earlier * onehot, axis=1)
    select = (slot_index[:, None] == jnp.arange(slots, dtype=jnp.int32)[None, :]).astype(
        jnp.bfloat16
    )
    select_tk = select.reshape(tok_rows, top_count, slots)
    select_tok = jnp.sum(select_tk, axis=1)
    grad_in = out_grad.astype(jnp.float32)
    grad_rows = (gate_probs[:, :, None] * grad_in[:, None, :]).astype(jnp.bfloat16)
    sel_tok3 = select_tok.reshape(tok_rows, devices_all, capacity)
    sel_tk3 = select_tk.reshape(tok_rows, top_count, devices_all, capacity)
    send_scaled = lax.dot_general(sel_tok3, scaled, (((0,), (0,)), ((), ())), preferred_element_type=jnp.float32).astype(jnp.bfloat16)
    send_grad = lax.dot_general(
        sel_tk3, grad_rows, (((0, 1), (0, 1)), ((), ())), preferred_element_type=jnp.float32
    ).astype(jnp.bfloat16)
    sent = jnp.concatenate([send_scaled, send_grad], axis=2)
    arrived_all = exchange(sent).reshape(slots, 2 * width)
    arrived = arrived_all[:, :width]
    arrived_grad = arrived_all[:, width:]
    expert_out, grad_back, grad_gate, grad_up, grad_down = expert_pass(
        arrived, arrived_grad, w_gate[0], w_up[0], w_down[0]
    )
    back = jnp.concatenate([expert_out, grad_back], axis=1).reshape(
        devices_all, capacity, 2 * width
    )
    returned, grad_gate, grad_up, grad_down = lax.optimization_barrier(
        (exchange(back), grad_gate, grad_up, grad_down)
    )
    returned = returned.reshape(slots, 2 * width)
    picked = [
        contract(select_tk[:, k, :], returned, 1, 0) for k in range(top_count)
    ]
    outs = [p[:, :width] for p in picked]
    backs = [p[:, width:] for p in picked]
    combined = gate_probs[:, 0:1] * outs[0]
    for k in range(1, top_count):
        combined = combined + gate_probs[:, k : k + 1] * outs[k]
    mixed = (inputs + combined).astype(jnp.bfloat16)
    grad_probs = jnp.stack([jnp.sum(grad_in * o, axis=1) for o in outs], axis=1)
    grad_normed = backs[0]
    for k in range(1, top_count):
        grad_normed = grad_normed + backs[k]
    gain_part = jnp.sum(grad_normed * normed, axis=0)
    grad_gain = all_sum(gain_part, devices_all)
    grad_scaled = grad_normed * norm_gain
    grad_tokens = (
        grad_in
        + inverse_rms
        * (grad_scaled - normed * jnp.mean(grad_scaled * normed, axis=1, keepdims=True))
    ).astype(jnp.bfloat16)
    return (
        mixed,
        grad_probs,
        grad_gain,
        grad_tokens,
        grad_gate[None],
        grad_up[None],
        grad_down[None],
    )


def solution(mesh):
    rows = P(AXES, None)
    stacked = P(AXES, None, None)
    return jax.shard_map(
        on_device,
        mesh=mesh,
        in_specs=(rows, rows, rows, P(), stacked, stacked, stacked, rows),
        out_specs=(rows, rows, P(), rows, stacked, stacked, stacked),
        check_vma=False,
    )
```

```python
import jax
import jax.numpy as jnp
from jax import lax
from jax.sharding import PartitionSpec as P

AXES = ("expert", "dp")


def exchange(rows):
    return lax.all_to_all(rows, AXES, split_axis=0, concat_axis=0, tiled=True)


def contract(left, right, left_dim, right_dim):
    return lax.dot_general(
        left, right, (((left_dim,), (right_dim,)), ((), ())), preferred_element_type=jnp.float32
    )


def all_sum(part, devices_all):
    me = lax.axis_index(AXES)
    total = part
    step = 1
    while step < devices_all:
        radix = 4 if step * 4 <= devices_all else 2
        held = [total] + [
            lax.ppermute(total, AXES, [(i, i ^ (x * step)) for i in range(devices_all)])
            for x in range(1, radix)
        ]
        position = (me // step) % radix
        canon = [lax.select_n(position ^ q, *held) for q in range(radix)]
        if radix == 4:
            total = (canon[0] + canon[1]) + (canon[2] + canon[3])
        else:
            total = canon[0] + canon[1]
        step *= radix
    return total


def expert_pass(arrived, arrived_grad, gate_matrix, up_matrix, down_matrix):
    pre_gate = jnp.dot(arrived, gate_matrix, preferred_element_type=jnp.float32)
    up_value = jnp.dot(arrived, up_matrix, preferred_element_type=jnp.float32)
    sigmoid_gate = jax.nn.sigmoid(pre_gate)
    activated = pre_gate * sigmoid_gate
    hidden = (activated * up_value).astype(jnp.bfloat16)
    expert_out = jnp.dot(hidden, down_matrix, preferred_element_type=jnp.float32).astype(
        jnp.bfloat16
    )
    grad_hidden = contract(arrived_grad, down_matrix, 1, 1)
    grad_down = contract(hidden, arrived_grad, 0, 0).astype(jnp.bfloat16)
    grad_pre = (
        grad_hidden * up_value * sigmoid_gate * (1.0 + pre_gate * (1.0 - sigmoid_gate))
    ).astype(jnp.bfloat16)
    grad_upval = (grad_hidden * activated).astype(jnp.bfloat16)
    grad_back = (
        contract(grad_pre, gate_matrix, 1, 1) + contract(grad_upval, up_matrix, 1, 1)
    ).astype(jnp.bfloat16)
    grad_gate = contract(arrived, grad_pre, 0, 0).astype(jnp.bfloat16)
    grad_up = contract(arrived, grad_upval, 0, 0).astype(jnp.bfloat16)
    return expert_out, grad_back, grad_gate, grad_up, grad_down


def on_device(tokens, routes, gate_probs, norm_gain, w_gate, w_up, w_down, out_grad):
    devices_all = lax.axis_size(AXES)
    tok_rows, width = tokens.shape
    top_count = routes.shape[1]
    assigned = tok_rows * top_count
    capacity = 2 * assigned // devices_all
    slots = devices_all * capacity
    inputs = tokens.astype(jnp.float32)
    inverse_rms = lax.rsqrt(jnp.mean(inputs * inputs, axis=1, keepdims=True) + 1e-06)
    normed = inputs * inverse_rms
    scaled = (normed * norm_gain).astype(jnp.bfloat16)
    flat_ids = routes.reshape(assigned)
    onehot = (flat_ids[:, None] == jnp.arange(devices_all, dtype=jnp.int32)[None, :]).astype(
        jnp.int32
    )
    earlier = jnp.cumsum(onehot, axis=0) - onehot
    slot_index = flat_ids * capacity + jnp.sum(earlier * onehot, axis=1)
    select = (slot_index[:, None] == jnp.arange(slots, dtype=jnp.int32)[None, :]).astype(
        jnp.bfloat16
    )
    select_tk = select.reshape(tok_rows, top_count, slots)
    select_tok = jnp.sum(select_tk, axis=1)
    grad_in = out_grad.astype(jnp.float32)
    grad_rows = (gate_probs[:, :, None] * grad_in[:, None, :]).astype(jnp.bfloat16)
    sel_tok3 = select_tok.reshape(tok_rows, devices_all, capacity)
    sel_tk3 = select_tk.reshape(tok_rows, top_count, devices_all, capacity)
    send_scaled = lax.dot_general(sel_tok3, scaled, (((0,), (0,)), ((), ())), preferred_element_type=jnp.float32).astype(jnp.bfloat16)
    send_grad = lax.dot_general(
        sel_tk3, grad_rows, (((0, 1), (0, 1)), ((), ())), preferred_element_type=jnp.float32
    ).astype(jnp.bfloat16)
    sent = jnp.concatenate([send_scaled, send_grad], axis=2)
    arrived_all = exchange(sent).reshape(slots, 2 * width)
    arrived = arrived_all[:, :width]
    arrived_grad = arrived_all[:, width:]
    expert_out, grad_back, grad_gate, grad_up, grad_down = expert_pass(
        arrived, arrived_grad, w_gate[0], w_up[0], w_down[0]
    )
    returned_grad, grad_gate, grad_up, grad_down = lax.optimization_barrier(
        (exchange(grad_back.reshape(devices_all, capacity, width)), grad_gate, grad_up, grad_down)
    )
    returned_grad = returned_grad.reshape(slots, width)
    returned_grad, expert_out = lax.optimization_barrier((returned_grad, expert_out))
    returned = exchange(expert_out.reshape(devices_all, capacity, width)).reshape(slots, width)
    backs = [contract(select_tk[:, k, :], returned_grad, 1, 0) for k in range(top_count)]
    outs = [contract(select_tk[:, k, :], returned, 1, 0) for k in range(top_count)]
    grad_normed = backs[0]
    for k in range(1, top_count):
        grad_normed = grad_normed + backs[k]
    combined = gate_probs[:, 0:1] * outs[0]
    for k in range(1, top_count):
        combined = combined + gate_probs[:, k : k + 1] * outs[k]
    mixed = (inputs + combined).astype(jnp.bfloat16)
    grad_probs = jnp.stack([jnp.sum(grad_in * o, axis=1) for o in outs], axis=1)
    gain_part = jnp.sum(grad_normed * normed, axis=0)
    grad_gain = all_sum(gain_part, devices_all)
    grad_scaled = grad_normed * norm_gain
    grad_tokens = (
        grad_in
        + inverse_rms
        * (grad_scaled - normed * jnp.mean(grad_scaled * normed, axis=1, keepdims=True))
    ).astype(jnp.bfloat16)
    return (
        mixed,
        grad_probs,
        grad_gain,
        grad_tokens,
        grad_gate[None],
        grad_up[None],
        grad_down[None],
    )


def solution(mesh):
    rows = P(AXES, None)
    stacked = P(AXES, None, None)
    return jax.shard_map(
        on_device,
        mesh=mesh,
        in_specs=(rows, rows, rows, P(), stacked, stacked, stacked, rows),
        out_specs=(rows, rows, P(), rows, stacked, stacked, stacked),
        check_vma=False,
    )
```

```python
import jax
import jax.numpy as jnp
from jax import lax
from jax.sharding import PartitionSpec as P

AXES = ("expert", "dp")


def exchange(rows):
    return lax.all_to_all(rows, AXES, split_axis=0, concat_axis=0, tiled=True)


def contract(left, right, left_dim, right_dim):
    return lax.dot_general(
        left, right, (((left_dim,), (right_dim,)), ((), ())), preferred_element_type=jnp.float32
    )


def all_sum(part, devices_all):
    me = lax.axis_index(AXES)
    total = part
    step = 1
    while step < devices_all:
        radix = 4 if step * 4 <= devices_all else 2
        held = [total] + [
            lax.ppermute(total, AXES, [(i, i ^ (x * step)) for i in range(devices_all)])
            for x in range(1, radix)
        ]
        position = (me // step) % radix
        canon = [lax.select_n(position ^ q, *held) for q in range(radix)]
        if radix == 4:
            total = (canon[0] + canon[1]) + (canon[2] + canon[3])
        else:
            total = canon[0] + canon[1]
        step *= radix
    return total


def expert_pass(arrived, arrived_grad, gate_matrix, up_matrix, down_matrix):
    pre_gate = jnp.dot(arrived, gate_matrix, preferred_element_type=jnp.float32)
    up_value = jnp.dot(arrived, up_matrix, preferred_element_type=jnp.float32)
    sigmoid_gate = jax.nn.sigmoid(pre_gate)
    activated = pre_gate * sigmoid_gate
    hidden = (activated * up_value).astype(jnp.bfloat16)
    expert_out = jnp.dot(hidden, down_matrix, preferred_element_type=jnp.float32).astype(
        jnp.bfloat16
    )
    grad_hidden = contract(arrived_grad, down_matrix, 1, 1)
    grad_down = contract(hidden, arrived_grad, 0, 0).astype(jnp.bfloat16)
    grad_pre = (
        grad_hidden * up_value * sigmoid_gate * (1.0 + pre_gate * (1.0 - sigmoid_gate))
    ).astype(jnp.bfloat16)
    grad_upval = (grad_hidden * activated).astype(jnp.bfloat16)
    grad_back = (
        contract(grad_pre, gate_matrix, 1, 1) + contract(grad_upval, up_matrix, 1, 1)
    ).astype(jnp.bfloat16)
    grad_gate = contract(arrived, grad_pre, 0, 0).astype(jnp.bfloat16)
    grad_up = contract(arrived, grad_upval, 0, 0).astype(jnp.bfloat16)
    return expert_out, grad_back, grad_gate, grad_up, grad_down


def on_device(tokens, routes, gate_probs, norm_gain, w_gate, w_up, w_down, out_grad):
    devices_all = lax.axis_size(AXES)
    tok_rows, width = tokens.shape
    top_count = routes.shape[1]
    assigned = tok_rows * top_count
    capacity = 2 * assigned // devices_all
    slots = devices_all * capacity
    inputs = tokens.astype(jnp.float32)
    inverse_rms = lax.rsqrt(jnp.mean(inputs * inputs, axis=1, keepdims=True) + 1e-06)
    normed = inputs * inverse_rms
    flat_ids = routes.reshape(assigned)
    onehot = (flat_ids[:, None] == jnp.arange(devices_all, dtype=jnp.int32)[None, :]).astype(
        jnp.int32
    )
    earlier = jnp.cumsum(onehot, axis=0) - onehot
    slot_index = flat_ids * capacity + jnp.sum(earlier * onehot, axis=1)
    select = (slot_index[:, None] == jnp.arange(slots, dtype=jnp.int32)[None, :]).astype(
        jnp.bfloat16
    )
    select_tk = select.reshape(tok_rows, top_count, slots)
    select_tok = jnp.sum(select_tk, axis=1)
    grad_in = out_grad.astype(jnp.float32)
    grad_rows = (gate_probs[:, :, None] * grad_in[:, None, :]).astype(jnp.bfloat16)
    sel_tok3 = select_tok.reshape(tok_rows, devices_all, capacity)
    sel_tk3 = select_tk.reshape(tok_rows, top_count, devices_all, capacity)
    send_scaled = lax.dot_general(sel_tok3, tokens, (((0,), (0,)), ((), ())), preferred_element_type=jnp.float32).astype(jnp.bfloat16)
    send_grad = lax.dot_general(
        sel_tk3, grad_rows, (((0, 1), (0, 1)), ((), ())), preferred_element_type=jnp.float32
    ).astype(jnp.bfloat16)
    sent = jnp.concatenate([send_scaled, send_grad], axis=2)
    arrived_all = exchange(sent).reshape(slots, 2 * width)
    arrived_inputs = arrived_all[:, :width].astype(jnp.float32)
    arrived_rms = lax.rsqrt(
        jnp.mean(arrived_inputs * arrived_inputs, axis=1, keepdims=True) + 1e-06
    )
    arrived_normed = arrived_inputs * arrived_rms
    arrived = (arrived_normed * norm_gain).astype(jnp.bfloat16)
    arrived_grad = arrived_all[:, width:]
    expert_out, grad_back, grad_gate, grad_up, grad_down = expert_pass(
        arrived, arrived_grad, w_gate[0], w_up[0], w_down[0]
    )
    grad_gain = all_sum(
        jnp.sum(grad_back.astype(jnp.float32) * arrived_normed, axis=0), devices_all
    )
    back = jnp.concatenate([expert_out, grad_back], axis=1).reshape(
        devices_all, capacity, 2 * width
    )
    returned, grad_gate, grad_up, grad_down = lax.optimization_barrier(
        (exchange(back), grad_gate, grad_up, grad_down)
    )
    returned = returned.reshape(slots, 2 * width)
    picked = [
        contract(select_tk[:, k, :], returned, 1, 0) for k in range(top_count)
    ]
    outs = [p[:, :width] for p in picked]
    backs = [p[:, width:] for p in picked]
    combined = gate_probs[:, 0:1] * outs[0]
    for k in range(1, top_count):
        combined = combined + gate_probs[:, k : k + 1] * outs[k]
    mixed = (inputs + combined).astype(jnp.bfloat16)
    grad_probs = jnp.stack([jnp.sum(grad_in * o, axis=1) for o in outs], axis=1)
    grad_normed = backs[0]
    for k in range(1, top_count):
        grad_normed = grad_normed + backs[k]
    grad_scaled = grad_normed * norm_gain
    grad_tokens = (
        grad_in
        + inverse_rms
        * (grad_scaled - normed * jnp.mean(grad_scaled * normed, axis=1, keepdims=True))
    ).astype(jnp.bfloat16)
    return (
        mixed,
        grad_probs,
        grad_gain,
        grad_tokens,
        grad_gate[None],
        grad_up[None],
        grad_down[None],
    )


def solution(mesh):
    rows = P(AXES, None)
    stacked = P(AXES, None, None)
    return jax.shard_map(
        on_device,
        mesh=mesh,
        in_specs=(rows, rows, rows, P(), stacked, stacked, stacked, rows),
        out_specs=(rows, rows, P(), rows, stacked, stacked, stacked),
        check_vma=False,
    )
```

```python
import jax
import jax.numpy as jnp
from jax import lax
from jax.sharding import PartitionSpec as P

AXES = ("expert", "dp")


def exchange(rows):
    return lax.all_to_all(rows, AXES, split_axis=0, concat_axis=0, tiled=True)


def contract(left, right, left_dim, right_dim):
    return lax.dot_general(
        left, right, (((left_dim,), (right_dim,)), ((), ())), preferred_element_type=jnp.float32
    )


def all_sum(part, devices_all):
    me = lax.axis_index(AXES)
    total = part
    step = 1
    while step < devices_all:
        radix = 4 if step * 4 <= devices_all else 2
        held = [total] + [
            lax.ppermute(total, AXES, [(i, i ^ (x * step)) for i in range(devices_all)])
            for x in range(1, radix)
        ]
        position = (me // step) % radix
        canon = [lax.select_n(position ^ q, *held) for q in range(radix)]
        if radix == 4:
            total = (canon[0] + canon[1]) + (canon[2] + canon[3])
        else:
            total = canon[0] + canon[1]
        step *= radix
    return total


def expert_pass(arrived, arrived_grad, gate_matrix, up_matrix, down_matrix):
    pre_gate = jnp.dot(arrived, gate_matrix, preferred_element_type=jnp.float32)
    up_value = jnp.dot(arrived, up_matrix, preferred_element_type=jnp.float32)
    sigmoid_gate = jax.nn.sigmoid(pre_gate)
    activated = pre_gate * sigmoid_gate
    hidden = (activated * up_value).astype(jnp.bfloat16)
    expert_out = jnp.dot(hidden, down_matrix, preferred_element_type=jnp.float32).astype(
        jnp.bfloat16
    )
    grad_hidden = contract(arrived_grad, down_matrix, 1, 1)
    grad_down = contract(hidden, arrived_grad, 0, 0).astype(jnp.bfloat16)
    grad_pre = (
        grad_hidden * up_value * sigmoid_gate * (1.0 + pre_gate * (1.0 - sigmoid_gate))
    ).astype(jnp.bfloat16)
    grad_upval = (grad_hidden * activated).astype(jnp.bfloat16)
    grad_back = (
        contract(grad_pre, gate_matrix, 1, 1) + contract(grad_upval, up_matrix, 1, 1)
    ).astype(jnp.bfloat16)
    grad_gate = contract(arrived, grad_pre, 0, 0).astype(jnp.bfloat16)
    grad_up = contract(arrived, grad_upval, 0, 0).astype(jnp.bfloat16)
    return expert_out, grad_back, grad_gate, grad_up, grad_down


def on_device(tokens, routes, gate_probs, norm_gain, w_gate, w_up, w_down, out_grad):
    devices_all = lax.axis_size(AXES)
    tok_rows, width = tokens.shape
    top_count = routes.shape[1]
    assigned = tok_rows * top_count
    capacity = 2 * assigned // devices_all
    slots = devices_all * capacity
    inputs = tokens.astype(jnp.float32)
    inverse_rms = lax.rsqrt(jnp.mean(inputs * inputs, axis=1, keepdims=True) + 1e-06)
    normed = inputs * inverse_rms
    flat_ids = routes.reshape(assigned)
    onehot = (flat_ids[:, None] == jnp.arange(devices_all, dtype=jnp.int32)[None, :]).astype(
        jnp.int32
    )
    earlier = jnp.cumsum(onehot, axis=0) - onehot
    slot_index = flat_ids * capacity + jnp.sum(earlier * onehot, axis=1)
    grad_in = out_grad.astype(jnp.float32)
    grad_rows = (gate_probs[:, :, None] * grad_in[:, None, :]).astype(jnp.bfloat16)
    lanes = jnp.arange(2 * slots, dtype=jnp.int32)[None, :]
    pair_slot = slot_index.reshape(tok_rows, top_count)
    token_pick = pair_slot[:, 0:1] * 2 == lanes
    for k in range(1, top_count):
        token_pick = token_pick | (pair_slot[:, k : k + 1] * 2 == lanes)
    grad_pick = slot_index[:, None] * 2 + 1 == lanes
    pick_send = jnp.concatenate([token_pick, grad_pick], axis=0).astype(jnp.bfloat16)
    source_rows = jnp.concatenate([tokens, grad_rows.reshape(assigned, width)], axis=0)
    sent = contract(pick_send, source_rows, 0, 0).astype(jnp.bfloat16)
    arrived_all = exchange(sent.reshape(devices_all, 2 * capacity, width)).reshape(2 * slots, width)
    arrived_inputs = arrived_all[0::2].astype(jnp.float32)
    arrived_rms = lax.rsqrt(
        jnp.mean(arrived_inputs * arrived_inputs, axis=1, keepdims=True) + 1e-06
    )
    arrived_normed = arrived_inputs * arrived_rms
    arrived = (arrived_normed * norm_gain).astype(jnp.bfloat16)
    arrived_grad = arrived_all[1::2]
    expert_out, grad_back, grad_gate, grad_up, grad_down = expert_pass(
        arrived, arrived_grad, w_gate[0], w_up[0], w_down[0]
    )
    grad_gain = all_sum(
        jnp.sum(grad_back.astype(jnp.float32) * arrived_normed, axis=0), devices_all
    )
    zero = jnp.zeros((), jnp.bfloat16)
    back = lax.pad(expert_out, zero, ((0, 1, 1), (0, 0, 0))) + lax.pad(
        grad_back, zero, ((1, 0, 1), (0, 0, 0))
    )
    back, grad_gain = lax.optimization_barrier((back, grad_gain))
    returned = exchange(back.reshape(devices_all, 2 * capacity, width)).reshape(2 * slots, width)
    order = slot_index.reshape(tok_rows, top_count).T.reshape(assigned)
    pick_back = jnp.concatenate([order * 2, order * 2 + 1])[:, None] == lanes
    picked = contract(pick_back.astype(jnp.bfloat16), returned, 1, 0)
    outs = [picked[k * tok_rows : (k + 1) * tok_rows] for k in range(top_count)]
    backs = [picked[(top_count + k) * tok_rows : (top_count + k + 1) * tok_rows] for k in range(top_count)]
    combined = gate_probs[:, 0:1] * outs[0]
    for k in range(1, top_count):
        combined = combined + gate_probs[:, k : k + 1] * outs[k]
    mixed = (inputs + combined).astype(jnp.bfloat16)
    grad_probs = jnp.stack([jnp.sum(grad_in * o, axis=1) for o in outs], axis=1)
    grad_normed = backs[0]
    for k in range(1, top_count):
        grad_normed = grad_normed + backs[k]
    grad_scaled = grad_normed * norm_gain
    grad_tokens = (
        grad_in
        + inverse_rms
        * (grad_scaled - normed * jnp.mean(grad_scaled * normed, axis=1, keepdims=True))
    ).astype(jnp.bfloat16)
    return (
        mixed,
        grad_probs,
        grad_gain,
        grad_tokens,
        grad_gate[None],
        grad_up[None],
        grad_down[None],
    )


def solution(mesh):
    rows = P(AXES, None)
    stacked = P(AXES, None, None)
    return jax.shard_map(
        on_device,
        mesh=mesh,
        in_specs=(rows, rows, rows, P(), stacked, stacked, stacked, rows),
        out_specs=(rows, rows, P(), rows, stacked, stacked, stacked),
        check_vma=False,
    )
```

```python
import jax
import jax.numpy as jnp
from jax import lax
from jax.sharding import PartitionSpec as P

AXES = ("expert", "dp")


def exchange(rows):
    return lax.all_to_all(rows, AXES, split_axis=0, concat_axis=0, tiled=True)


def contract(left, right, left_dim, right_dim):
    return lax.dot_general(
        left, right, (((left_dim,), (right_dim,)), ((), ())), preferred_element_type=jnp.float32
    )


def all_sum(part, devices_all):
    me = lax.axis_index(AXES)
    total = part
    step = 1
    while step < devices_all:
        radix = 4 if step * 4 <= devices_all else 2
        held = [total] + [
            lax.ppermute(total, AXES, [(i, i ^ (x * step)) for i in range(devices_all)])
            for x in range(1, radix)
        ]
        position = (me // step) % radix
        canon = [lax.select_n(position ^ q, *held) for q in range(radix)]
        if radix == 4:
            total = (canon[0] + canon[1]) + (canon[2] + canon[3])
        else:
            total = canon[0] + canon[1]
        step *= radix
    return total


def expert_pass(arrived, arrived_grad, gate_matrix, up_matrix, down_matrix):
    pre_gate = jnp.dot(arrived, gate_matrix, preferred_element_type=jnp.float32)
    up_value = jnp.dot(arrived, up_matrix, preferred_element_type=jnp.float32)
    sigmoid_gate = jax.nn.sigmoid(pre_gate)
    activated = pre_gate * sigmoid_gate
    hidden = (activated * up_value).astype(jnp.bfloat16)
    expert_out = jnp.dot(hidden, down_matrix, preferred_element_type=jnp.float32).astype(
        jnp.bfloat16
    )
    grad_hidden = contract(arrived_grad, down_matrix, 1, 1)
    grad_down = contract(hidden, arrived_grad, 0, 0).astype(jnp.bfloat16)
    grad_pre = (
        grad_hidden * up_value * sigmoid_gate * (1.0 + pre_gate * (1.0 - sigmoid_gate))
    ).astype(jnp.bfloat16)
    grad_upval = (grad_hidden * activated).astype(jnp.bfloat16)
    grad_back = (
        contract(grad_pre, gate_matrix, 1, 1) + contract(grad_upval, up_matrix, 1, 1)
    ).astype(jnp.bfloat16)
    grad_gate = contract(arrived, grad_pre, 0, 0).astype(jnp.bfloat16)
    grad_up = contract(arrived, grad_upval, 0, 0).astype(jnp.bfloat16)
    return expert_out, grad_back, grad_gate, grad_up, grad_down


def on_device(tokens, routes, gate_probs, norm_gain, w_gate, w_up, w_down, out_grad):
    devices_all = lax.axis_size(AXES)
    tok_rows, width = tokens.shape
    top_count = routes.shape[1]
    assigned = tok_rows * top_count
    capacity = 2 * assigned // devices_all
    slots = devices_all * capacity
    inputs = tokens.astype(jnp.float32)
    inverse_rms = lax.rsqrt(jnp.mean(inputs * inputs, axis=1, keepdims=True) + 1e-06)
    normed = inputs * inverse_rms
    flat_ids = routes.reshape(assigned)
    onehot = (flat_ids[:, None] == jnp.arange(devices_all, dtype=jnp.int32)[None, :]).astype(
        jnp.int32
    )
    earlier = jnp.cumsum(onehot, axis=0) - onehot
    slot_index = flat_ids * capacity + jnp.sum(earlier * onehot, axis=1)
    select = (slot_index[:, None] == jnp.arange(slots, dtype=jnp.int32)[None, :]).astype(
        jnp.bfloat16
    )
    select_tk = select.reshape(tok_rows, top_count, slots)
    select_tok = jnp.sum(select_tk, axis=1)
    grad_in = out_grad.astype(jnp.float32)
    grad_rows = (gate_probs[:, :, None] * grad_in[:, None, :]).astype(jnp.bfloat16)
    sel_tok3 = select_tok.reshape(tok_rows, devices_all, capacity)
    sel_tk3 = select_tk.reshape(tok_rows, top_count, devices_all, capacity)
    send_scaled = lax.dot_general(sel_tok3, tokens, (((0,), (0,)), ((), ())), preferred_element_type=jnp.float32).astype(jnp.bfloat16)
    send_grad = lax.dot_general(
        sel_tk3, grad_rows, (((0, 1), (0, 1)), ((), ())), preferred_element_type=jnp.float32
    ).astype(jnp.bfloat16)
    sent = jnp.concatenate([send_scaled, send_grad], axis=2)
    arrived_all = exchange(sent).reshape(slots, 2 * width)
    arrived_inputs = arrived_all[:, :width].astype(jnp.float32)
    arrived_rms = lax.rsqrt(
        jnp.mean(arrived_inputs * arrived_inputs, axis=1, keepdims=True) + 1e-06
    )
    arrived_normed = arrived_inputs * arrived_rms
    arrived = (arrived_normed * norm_gain).astype(jnp.bfloat16)
    arrived_grad = arrived_all[:, width:]
    expert_out, grad_back, grad_gate, grad_up, grad_down = expert_pass(
        arrived, arrived_grad, w_gate[0], w_up[0], w_down[0]
    )
    grad_gain = all_sum(
        jnp.sum(grad_back.astype(jnp.float32) * arrived_normed, axis=0), devices_all
    )
    back = jnp.concatenate([expert_out, grad_back], axis=1).reshape(
        devices_all, capacity, 2 * width
    )
    back, grad_gain = lax.optimization_barrier((back, grad_gain))
    returned, grad_gate, grad_up, grad_down = lax.optimization_barrier(
        (exchange(back), grad_gate, grad_up, grad_down)
    )
    returned = returned.reshape(slots, 2 * width)
    picked = [
        contract(select_tk[:, k, :], returned, 1, 0) for k in range(top_count)
    ]
    outs = [p[:, :width] for p in picked]
    backs = [p[:, width:] for p in picked]
    combined = gate_probs[:, 0:1] * outs[0]
    for k in range(1, top_count):
        combined = combined + gate_probs[:, k : k + 1] * outs[k]
    mixed = (inputs + combined).astype(jnp.bfloat16)
    grad_probs = jnp.stack([jnp.sum(grad_in * o, axis=1) for o in outs], axis=1)
    grad_normed = backs[0]
    for k in range(1, top_count):
        grad_normed = grad_normed + backs[k]
    grad_scaled = grad_normed * norm_gain
    grad_tokens = (
        grad_in
        + inverse_rms
        * (grad_scaled - normed * jnp.mean(grad_scaled * normed, axis=1, keepdims=True))
    ).astype(jnp.bfloat16)
    return (
        mixed,
        grad_probs,
        grad_gain,
        grad_tokens,
        grad_gate[None],
        grad_up[None],
        grad_down[None],
    )


def solution(mesh):
    rows = P(AXES, None)
    stacked = P(AXES, None, None)
    return jax.shard_map(
        on_device,
        mesh=mesh,
        in_specs=(rows, rows, rows, P(), stacked, stacked, stacked, rows),
        out_specs=(rows, rows, P(), rows, stacked, stacked, stacked),
        check_vma=False,
    )
```

```python
import jax
import jax.numpy as jnp
from jax import lax
from jax.sharding import PartitionSpec as P

AXES = ("expert", "dp")


def exchange(rows):
    return lax.all_to_all(rows, AXES, split_axis=0, concat_axis=0, tiled=True)


def contract(left, right, left_dim, right_dim):
    return lax.dot_general(
        left, right, (((left_dim,), (right_dim,)), ((), ())), preferred_element_type=jnp.float32
    )


def all_sum(part, devices_all):
    me = lax.axis_index(AXES)
    total = part
    step = 1
    while step < devices_all:
        radix = 4 if step * 4 <= devices_all else 2
        held = [total] + [
            lax.ppermute(total, AXES, [(i, i ^ (x * step)) for i in range(devices_all)])
            for x in range(1, radix)
        ]
        position = (me // step) % radix
        canon = [lax.select_n(position ^ q, *held) for q in range(radix)]
        if radix == 4:
            total = (canon[0] + canon[1]) + (canon[2] + canon[3])
        else:
            total = canon[0] + canon[1]
        step *= radix
    return total


def expert_pass(arrived, arrived_grad, gate_matrix, up_matrix, down_matrix):
    pre_gate = jnp.dot(arrived, gate_matrix, preferred_element_type=jnp.float32)
    up_value = jnp.dot(arrived, up_matrix, preferred_element_type=jnp.float32)
    sigmoid_gate = jax.nn.sigmoid(pre_gate)
    activated = pre_gate * sigmoid_gate
    hidden = (activated * up_value).astype(jnp.bfloat16)
    expert_out = jnp.dot(hidden, down_matrix, preferred_element_type=jnp.float32).astype(
        jnp.bfloat16
    )
    grad_hidden = contract(arrived_grad, down_matrix, 1, 1)
    grad_down = contract(hidden, arrived_grad, 0, 0).astype(jnp.bfloat16)
    grad_pre = (
        grad_hidden * up_value * sigmoid_gate * (1.0 + pre_gate * (1.0 - sigmoid_gate))
    ).astype(jnp.bfloat16)
    grad_upval = (grad_hidden * activated).astype(jnp.bfloat16)
    grad_back = (
        contract(grad_pre, gate_matrix, 1, 1) + contract(grad_upval, up_matrix, 1, 1)
    ).astype(jnp.bfloat16)
    grad_gate = contract(arrived, grad_pre, 0, 0).astype(jnp.bfloat16)
    grad_up = contract(arrived, grad_upval, 0, 0).astype(jnp.bfloat16)
    return expert_out, grad_back, grad_gate, grad_up, grad_down


def on_device(tokens, routes, gate_probs, norm_gain, w_gate, w_up, w_down, out_grad):
    devices_all = lax.axis_size(AXES)
    tok_rows, width = tokens.shape
    top_count = routes.shape[1]
    assigned = tok_rows * top_count
    capacity = 2 * assigned // devices_all
    slots = devices_all * capacity
    inputs = tokens.astype(jnp.float32)
    inverse_rms = lax.rsqrt(jnp.mean(inputs * inputs, axis=1, keepdims=True) + 1e-06)
    normed = inputs * inverse_rms
    flat_ids = routes.reshape(assigned)
    onehot = (flat_ids[:, None] == jnp.arange(devices_all, dtype=jnp.int32)[None, :]).astype(
        jnp.int32
    )
    earlier = jnp.cumsum(onehot, axis=0) - onehot
    slot_index = flat_ids * capacity + jnp.sum(earlier * onehot, axis=1)
    select = (slot_index[:, None] == jnp.arange(slots, dtype=jnp.int32)[None, :]).astype(
        jnp.bfloat16
    )
    select_tk = select.reshape(tok_rows, top_count, slots)
    select_tok = jnp.sum(select_tk, axis=1)
    grad_in = out_grad.astype(jnp.float32)
    grad_rows = (gate_probs[:, :, None] * grad_in[:, None, :]).astype(jnp.bfloat16)
    sel_tok3 = select_tok.reshape(tok_rows, devices_all, capacity)
    sel_tk3 = select_tk.reshape(tok_rows, top_count, devices_all, capacity)
    send_scaled = lax.dot_general(sel_tok3, tokens, (((0,), (0,)), ((), ())), preferred_element_type=jnp.float32).astype(jnp.bfloat16)
    send_grad = lax.dot_general(
        sel_tk3, grad_rows, (((0, 1), (0, 1)), ((), ())), preferred_element_type=jnp.float32
    ).astype(jnp.bfloat16)
    sent = jnp.concatenate([send_scaled, send_grad], axis=2)
    arrived_all = exchange(sent).reshape(slots, 2 * width)
    arrived_inputs = arrived_all[:, :width].astype(jnp.float32)
    arrived_rms = lax.rsqrt(
        jnp.mean(arrived_inputs * arrived_inputs, axis=1, keepdims=True) + 1e-06
    )
    arrived_normed = arrived_inputs * arrived_rms
    arrived = (arrived_normed * norm_gain).astype(jnp.bfloat16)
    arrived_grad = arrived_all[:, width:]
    expert_out, grad_back, grad_gate, grad_up, grad_down = expert_pass(
        arrived, arrived_grad, w_gate[0], w_up[0], w_down[0]
    )
    gain_part = jnp.sum(grad_back.astype(jnp.float32) * arrived_normed, axis=0)
    back = jnp.concatenate([expert_out, grad_back], axis=1).reshape(
        devices_all, capacity, 2 * width
    )
    returned, grad_gate, grad_up, grad_down, gain_part = lax.optimization_barrier(
        (exchange(back), grad_gate, grad_up, grad_down, gain_part)
    )
    grad_gain = all_sum(gain_part, devices_all)
    returned = returned.reshape(slots, 2 * width)
    picked = [
        contract(select_tk[:, k, :], returned, 1, 0) for k in range(top_count)
    ]
    outs = [p[:, :width] for p in picked]
    backs = [p[:, width:] for p in picked]
    combined = gate_probs[:, 0:1] * outs[0]
    for k in range(1, top_count):
        combined = combined + gate_probs[:, k : k + 1] * outs[k]
    mixed = (inputs + combined).astype(jnp.bfloat16)
    grad_probs = jnp.stack([jnp.sum(grad_in * o, axis=1) for o in outs], axis=1)
    grad_normed = backs[0]
    for k in range(1, top_count):
        grad_normed = grad_normed + backs[k]
    grad_scaled = grad_normed * norm_gain
    grad_tokens = (
        grad_in
        + inverse_rms
        * (grad_scaled - normed * jnp.mean(grad_scaled * normed, axis=1, keepdims=True))
    ).astype(jnp.bfloat16)
    return (
        mixed,
        grad_probs,
        grad_gain,
        grad_tokens,
        grad_gate[None],
        grad_up[None],
        grad_down[None],
    )


def solution(mesh):
    rows = P(AXES, None)
    stacked = P(AXES, None, None)
    return jax.shard_map(
        on_device,
        mesh=mesh,
        in_specs=(rows, rows, rows, P(), stacked, stacked, stacked, rows),
        out_specs=(rows, rows, P(), rows, stacked, stacked, stacked),
        check_vma=False,
    )
```

```python
import jax
import jax.numpy as jnp
from jax import lax
from jax.sharding import PartitionSpec as P

AXES = ("expert", "dp")


def exchange(rows):
    return lax.all_to_all(rows, AXES, split_axis=0, concat_axis=0, tiled=True)


def contract(left, right, left_dim, right_dim):
    return lax.dot_general(
        left, right, (((left_dim,), (right_dim,)), ((), ())), preferred_element_type=jnp.float32
    )


def all_sum(part, devices_all):
    me = lax.axis_index(AXES)
    total = part
    step = 1
    while step < devices_all:
        radix = 4 if step * 4 <= devices_all else 2
        held = [total] + [
            lax.ppermute(total, AXES, [(i, i ^ (x * step)) for i in range(devices_all)])
            for x in range(1, radix)
        ]
        position = (me // step) % radix
        canon = [lax.select_n(position ^ q, *held) for q in range(radix)]
        if radix == 4:
            total = (canon[0] + canon[1]) + (canon[2] + canon[3])
        else:
            total = canon[0] + canon[1]
        step *= radix
    return total


def expert_pass(arrived, arrived_grad, gate_matrix, up_matrix, down_matrix):
    pre_gate = jnp.dot(arrived, gate_matrix, preferred_element_type=jnp.float32)
    up_value = jnp.dot(arrived, up_matrix, preferred_element_type=jnp.float32)
    sigmoid_gate = jax.nn.sigmoid(pre_gate)
    activated = pre_gate * sigmoid_gate
    hidden = (activated * up_value).astype(jnp.bfloat16)
    expert_out = jnp.dot(hidden, down_matrix, preferred_element_type=jnp.float32).astype(
        jnp.bfloat16
    )
    grad_hidden = contract(arrived_grad, down_matrix, 1, 1)
    grad_down = contract(hidden, arrived_grad, 0, 0).astype(jnp.bfloat16)
    grad_pre = (
        grad_hidden * up_value * sigmoid_gate * (1.0 + pre_gate * (1.0 - sigmoid_gate))
    ).astype(jnp.bfloat16)
    grad_upval = (grad_hidden * activated).astype(jnp.bfloat16)
    grad_back = (
        contract(grad_pre, gate_matrix, 1, 1) + contract(grad_upval, up_matrix, 1, 1)
    ).astype(jnp.bfloat16)
    grad_gate = contract(arrived, grad_pre, 0, 0).astype(jnp.bfloat16)
    grad_up = contract(arrived, grad_upval, 0, 0).astype(jnp.bfloat16)
    return expert_out, grad_back, grad_gate, grad_up, grad_down


def on_device(tokens, routes, gate_probs, norm_gain, w_gate, w_up, w_down, out_grad):
    devices_all = lax.axis_size(AXES)
    tok_rows, width = tokens.shape
    top_count = routes.shape[1]
    assigned = tok_rows * top_count
    capacity = 2 * assigned // devices_all
    slots = devices_all * capacity
    inputs = tokens.astype(jnp.float32)
    inverse_rms = lax.rsqrt(jnp.mean(inputs * inputs, axis=1, keepdims=True) + 1e-06)
    normed = inputs * inverse_rms
    flat_ids = routes.reshape(assigned)
    onehot = (flat_ids[:, None] == jnp.arange(devices_all, dtype=jnp.int32)[None, :]).astype(
        jnp.int32
    )
    earlier = jnp.cumsum(onehot, axis=0) - onehot
    slot_index = flat_ids * capacity + jnp.sum(earlier * onehot, axis=1)
    select = (slot_index[:, None] == jnp.arange(slots, dtype=jnp.int32)[None, :]).astype(
        jnp.bfloat16
    )
    select_tk = select.reshape(tok_rows, top_count, slots)
    select_tok = jnp.sum(select_tk, axis=1)
    grad_in = out_grad.astype(jnp.float32)
    grad_rows = (gate_probs[:, :, None] * grad_in[:, None, :]).astype(jnp.bfloat16)
    sel_tok3 = select_tok.reshape(tok_rows, devices_all, capacity)
    sel_tk3 = select_tk.reshape(tok_rows, top_count, devices_all, capacity)
    send_scaled = lax.dot_general(sel_tok3, tokens, (((0,), (0,)), ((), ())), preferred_element_type=jnp.float32).astype(jnp.bfloat16)
    send_grad = lax.dot_general(
        sel_tk3, grad_rows, (((0, 1), (0, 1)), ((), ())), preferred_element_type=jnp.float32
    ).astype(jnp.bfloat16)
    sent = jnp.concatenate([send_scaled, send_grad], axis=2)
    arrived_all = exchange(sent).reshape(slots, 2 * width)
    arrived_inputs = arrived_all[:, :width].astype(jnp.float32)
    arrived_rms = lax.rsqrt(
        jnp.mean(arrived_inputs * arrived_inputs, axis=1, keepdims=True) + 1e-06
    )
    arrived_normed = arrived_inputs * arrived_rms
    arrived = (arrived_normed * norm_gain).astype(jnp.bfloat16)
    arrived_grad = arrived_all[:, width:]
    expert_out, grad_back, grad_gate, grad_up, grad_down = expert_pass(
        arrived, arrived_grad, w_gate[0], w_up[0], w_down[0]
    )
    gain_part = jnp.sum(grad_back.astype(jnp.float32) * arrived_normed, axis=0)
    back = jnp.concatenate([expert_out, grad_back], axis=1).reshape(
        devices_all, capacity, 2 * width
    )
    returned, grad_gate, grad_up, grad_down, gain_part = lax.optimization_barrier(
        (exchange(back), grad_gate, grad_up, grad_down, gain_part)
    )
    grad_gain = all_sum(gain_part, devices_all)
    pair_slot = slot_index.reshape(tok_rows, top_count)
    picked = [
        returned[pair_slot[:, k] // capacity, pair_slot[:, k] % capacity].astype(jnp.float32)
        for k in range(top_count)
    ]
    outs = [p[:, :width] for p in picked]
    backs = [p[:, width:] for p in picked]
    combined = gate_probs[:, 0:1] * outs[0]
    for k in range(1, top_count):
        combined = combined + gate_probs[:, k : k + 1] * outs[k]
    mixed = (inputs + combined).astype(jnp.bfloat16)
    grad_probs = jnp.stack([jnp.sum(grad_in * o, axis=1) for o in outs], axis=1)
    grad_normed = backs[0]
    for k in range(1, top_count):
        grad_normed = grad_normed + backs[k]
    grad_scaled = grad_normed * norm_gain
    grad_tokens = (
        grad_in
        + inverse_rms
        * (grad_scaled - normed * jnp.mean(grad_scaled * normed, axis=1, keepdims=True))
    ).astype(jnp.bfloat16)
    return (
        mixed,
        grad_probs,
        grad_gain,
        grad_tokens,
        grad_gate[None],
        grad_up[None],
        grad_down[None],
    )


def solution(mesh):
    rows = P(AXES, None)
    stacked = P(AXES, None, None)
    return jax.shard_map(
        on_device,
        mesh=mesh,
        in_specs=(rows, rows, rows, P(), stacked, stacked, stacked, rows),
        out_specs=(rows, rows, P(), rows, stacked, stacked, stacked),
        check_vma=False,
    )
```

```python
import jax
import jax.numpy as jnp
from jax import lax
from jax.sharding import PartitionSpec as P

AXES = ("expert", "dp")


def exchange(rows):
    return lax.all_to_all(rows, AXES, split_axis=0, concat_axis=0, tiled=True)


def contract(left, right, left_dim, right_dim):
    return lax.dot_general(
        left, right, (((left_dim,), (right_dim,)), ((), ())), preferred_element_type=jnp.float32
    )


def all_sum(part, devices_all):
    me = lax.axis_index(AXES)
    total = part
    step = 1
    while step < devices_all:
        radix = 2
        held = [total] + [
            lax.ppermute(total, AXES, [(i, i ^ (x * step)) for i in range(devices_all)])
            for x in range(1, radix)
        ]
        position = (me // step) % radix
        canon = [lax.select_n(position ^ q, *held) for q in range(radix)]
        if radix == 4:
            total = (canon[0] + canon[1]) + (canon[2] + canon[3])
        else:
            total = canon[0] + canon[1]
        step *= radix
    return total


def expert_pass(arrived, arrived_grad, gate_matrix, up_matrix, down_matrix):
    pre_gate = jnp.dot(arrived, gate_matrix, preferred_element_type=jnp.float32)
    up_value = jnp.dot(arrived, up_matrix, preferred_element_type=jnp.float32)
    sigmoid_gate = jax.nn.sigmoid(pre_gate)
    activated = pre_gate * sigmoid_gate
    hidden = (activated * up_value).astype(jnp.bfloat16)
    expert_out = jnp.dot(hidden, down_matrix, preferred_element_type=jnp.float32).astype(
        jnp.bfloat16
    )
    grad_hidden = contract(arrived_grad, down_matrix, 1, 1)
    grad_down = contract(hidden, arrived_grad, 0, 0).astype(jnp.bfloat16)
    grad_pre = (
        grad_hidden * up_value * sigmoid_gate * (1.0 + pre_gate * (1.0 - sigmoid_gate))
    ).astype(jnp.bfloat16)
    grad_upval = (grad_hidden * activated).astype(jnp.bfloat16)
    grad_back = (
        contract(grad_pre, gate_matrix, 1, 1) + contract(grad_upval, up_matrix, 1, 1)
    ).astype(jnp.bfloat16)
    grad_gate = contract(arrived, grad_pre, 0, 0).astype(jnp.bfloat16)
    grad_up = contract(arrived, grad_upval, 0, 0).astype(jnp.bfloat16)
    return expert_out, grad_back, grad_gate, grad_up, grad_down


def on_device(tokens, routes, gate_probs, norm_gain, w_gate, w_up, w_down, out_grad):
    devices_all = lax.axis_size(AXES)
    tok_rows, width = tokens.shape
    top_count = routes.shape[1]
    assigned = tok_rows * top_count
    capacity = 2 * assigned // devices_all
    slots = devices_all * capacity
    inputs = tokens.astype(jnp.float32)
    inverse_rms = lax.rsqrt(jnp.mean(inputs * inputs, axis=1, keepdims=True) + 1e-06)
    normed = inputs * inverse_rms
    flat_ids = routes.reshape(assigned)
    onehot = (flat_ids[:, None] == jnp.arange(devices_all, dtype=jnp.int32)[None, :]).astype(
        jnp.int32
    )
    earlier = jnp.cumsum(onehot, axis=0) - onehot
    slot_index = flat_ids * capacity + jnp.sum(earlier * onehot, axis=1)
    select = (slot_index[:, None] == jnp.arange(slots, dtype=jnp.int32)[None, :]).astype(
        jnp.bfloat16
    )
    select_tk = select.reshape(tok_rows, top_count, slots)
    select_tok = jnp.sum(select_tk, axis=1)
    grad_in = out_grad.astype(jnp.float32)
    grad_rows = (gate_probs[:, :, None] * grad_in[:, None, :]).astype(jnp.bfloat16)
    sel_tok3 = select_tok.reshape(tok_rows, devices_all, capacity)
    sel_tk3 = select_tk.reshape(tok_rows, top_count, devices_all, capacity)
    send_scaled = lax.dot_general(sel_tok3, tokens, (((0,), (0,)), ((), ())), preferred_element_type=jnp.float32).astype(jnp.bfloat16)
    send_grad = lax.dot_general(
        sel_tk3, grad_rows, (((0, 1), (0, 1)), ((), ())), preferred_element_type=jnp.float32
    ).astype(jnp.bfloat16)
    sent = jnp.concatenate([send_scaled, send_grad], axis=2)
    arrived_all = exchange(sent).reshape(slots, 2 * width)
    arrived_inputs = arrived_all[:, :width].astype(jnp.float32)
    arrived_rms = lax.rsqrt(
        jnp.mean(arrived_inputs * arrived_inputs, axis=1, keepdims=True) + 1e-06
    )
    arrived_normed = arrived_inputs * arrived_rms
    arrived = (arrived_normed * norm_gain).astype(jnp.bfloat16)
    arrived_grad = arrived_all[:, width:]
    expert_out, grad_back, grad_gate, grad_up, grad_down = expert_pass(
        arrived, arrived_grad, w_gate[0], w_up[0], w_down[0]
    )
    gain_part = jnp.sum(grad_back.astype(jnp.float32) * arrived_normed, axis=0)
    back = jnp.concatenate([expert_out, grad_back], axis=1).reshape(
        devices_all, capacity, 2 * width
    )
    returned, grad_gate, grad_up, grad_down, gain_part = lax.optimization_barrier(
        (exchange(back), grad_gate, grad_up, grad_down, gain_part)
    )
    grad_gain = all_sum(gain_part, devices_all)
    returned = returned.reshape(slots, 2 * width)
    picked = [
        contract(select_tk[:, k, :], returned, 1, 0) for k in range(top_count)
    ]
    outs = [p[:, :width] for p in picked]
    backs = [p[:, width:] for p in picked]
    combined = gate_probs[:, 0:1] * outs[0]
    for k in range(1, top_count):
        combined = combined + gate_probs[:, k : k + 1] * outs[k]
    mixed = (inputs + combined).astype(jnp.bfloat16)
    grad_probs = jnp.stack([jnp.sum(grad_in * o, axis=1) for o in outs], axis=1)
    grad_normed = backs[0]
    for k in range(1, top_count):
        grad_normed = grad_normed + backs[k]
    grad_scaled = grad_normed * norm_gain
    grad_tokens = (
        grad_in
        + inverse_rms
        * (grad_scaled - normed * jnp.mean(grad_scaled * normed, axis=1, keepdims=True))
    ).astype(jnp.bfloat16)
    return (
        mixed,
        grad_probs,
        grad_gain,
        grad_tokens,
        grad_gate[None],
        grad_up[None],
        grad_down[None],
    )


def solution(mesh):
    rows = P(AXES, None)
    stacked = P(AXES, None, None)
    return jax.shard_map(
        on_device,
        mesh=mesh,
        in_specs=(rows, rows, rows, P(), stacked, stacked, stacked, rows),
        out_specs=(rows, rows, P(), rows, stacked, stacked, stacked),
        check_vma=False,
    )
```

```python
import jax
import jax.numpy as jnp
from jax import lax
from jax.sharding import PartitionSpec as P

AXES = ("expert", "dp")


def exchange(rows):
    return lax.all_to_all(rows, AXES, split_axis=0, concat_axis=0, tiled=True)


def contract(left, right, left_dim, right_dim):
    return lax.dot_general(
        left, right, (((left_dim,), (right_dim,)), ((), ())), preferred_element_type=jnp.float32
    )


def all_sum(part, devices_all, steps):
    total = part
    for step in steps:
        pairs = [(i, i ^ step) for i in range(devices_all)]
        total = total + lax.ppermute(total, AXES, pairs)
    return total


def expert_pass(arrived, arrived_grad, gate_matrix, up_matrix, down_matrix):
    pre_gate = jnp.dot(arrived, gate_matrix, preferred_element_type=jnp.float32)
    up_value = jnp.dot(arrived, up_matrix, preferred_element_type=jnp.float32)
    sigmoid_gate = jax.nn.sigmoid(pre_gate)
    activated = pre_gate * sigmoid_gate
    hidden = (activated * up_value).astype(jnp.bfloat16)
    expert_out = jnp.dot(hidden, down_matrix, preferred_element_type=jnp.float32).astype(
        jnp.bfloat16
    )
    grad_hidden = contract(arrived_grad, down_matrix, 1, 1)
    grad_down = contract(hidden, arrived_grad, 0, 0).astype(jnp.bfloat16)
    grad_pre = (
        grad_hidden * up_value * sigmoid_gate * (1.0 + pre_gate * (1.0 - sigmoid_gate))
    ).astype(jnp.bfloat16)
    grad_upval = (grad_hidden * activated).astype(jnp.bfloat16)
    grad_back = (
        contract(grad_pre, gate_matrix, 1, 1) + contract(grad_upval, up_matrix, 1, 1)
    ).astype(jnp.bfloat16)
    grad_gate = contract(arrived, grad_pre, 0, 0).astype(jnp.bfloat16)
    grad_up = contract(arrived, grad_upval, 0, 0).astype(jnp.bfloat16)
    return expert_out, grad_back, grad_gate, grad_up, grad_down


def on_device(tokens, routes, gate_probs, norm_gain, w_gate, w_up, w_down, out_grad):
    devices_all = lax.axis_size(AXES)
    tok_rows, width = tokens.shape
    top_count = routes.shape[1]
    assigned = tok_rows * top_count
    capacity = 2 * assigned // devices_all
    slots = devices_all * capacity
    inputs = tokens.astype(jnp.float32)
    inverse_rms = lax.rsqrt(jnp.mean(inputs * inputs, axis=1, keepdims=True) + 1e-06)
    normed = inputs * inverse_rms
    flat_ids = routes.reshape(assigned)
    onehot = (flat_ids[:, None] == jnp.arange(devices_all, dtype=jnp.int32)[None, :]).astype(
        jnp.int32
    )
    earlier = jnp.cumsum(onehot, axis=0) - onehot
    slot_index = flat_ids * capacity + jnp.sum(earlier * onehot, axis=1)
    select = (slot_index[:, None] == jnp.arange(slots, dtype=jnp.int32)[None, :]).astype(
        jnp.bfloat16
    )
    select_tk = select.reshape(tok_rows, top_count, slots)
    select_tok = jnp.sum(select_tk, axis=1)
    grad_in = out_grad.astype(jnp.float32)
    grad_rows = (gate_probs[:, :, None] * grad_in[:, None, :]).astype(jnp.bfloat16)
    sel_tok3 = select_tok.reshape(tok_rows, devices_all, capacity)
    sel_tk3 = select_tk.reshape(tok_rows, top_count, devices_all, capacity)
    send_scaled = lax.dot_general(sel_tok3, tokens, (((0,), (0,)), ((), ())), preferred_element_type=jnp.float32).astype(jnp.bfloat16)
    send_grad = lax.dot_general(
        sel_tk3, grad_rows, (((0, 1), (0, 1)), ((), ())), preferred_element_type=jnp.float32
    ).astype(jnp.bfloat16)
    sent = jnp.concatenate([send_scaled, send_grad], axis=2)
    arrived_all = exchange(sent).reshape(slots, 2 * width)
    arrived_inputs = arrived_all[:, :width].astype(jnp.float32)
    arrived_rms = lax.rsqrt(
        jnp.mean(arrived_inputs * arrived_inputs, axis=1, keepdims=True) + 1e-06
    )
    arrived_normed = arrived_inputs * arrived_rms
    arrived = (arrived_normed * norm_gain).astype(jnp.bfloat16)
    arrived_grad = arrived_all[:, width:]
    expert_out, grad_back, grad_gate, grad_up, grad_down = expert_pass(
        arrived, arrived_grad, w_gate[0], w_up[0], w_down[0]
    )
    gain_part = jnp.sum(grad_back.astype(jnp.float32) * arrived_normed, axis=0)
    back = jnp.concatenate([expert_out, grad_back], axis=1).reshape(
        devices_all, capacity, 2 * width
    )
    bits = [1 << b for b in range(devices_all.bit_length() - 1)]
    gain_part = all_sum(gain_part, devices_all, bits[:3])
    back, gain_part = lax.optimization_barrier((back, gain_part))
    returned, grad_gate, grad_up, grad_down, gain_part = lax.optimization_barrier(
        (exchange(back), grad_gate, grad_up, grad_down, gain_part)
    )
    grad_gain = all_sum(gain_part, devices_all, bits[3:])
    returned = returned.reshape(slots, 2 * width)
    picked = [
        contract(select_tk[:, k, :], returned, 1, 0) for k in range(top_count)
    ]
    outs = [p[:, :width] for p in picked]
    backs = [p[:, width:] for p in picked]
    combined = gate_probs[:, 0:1] * outs[0]
    for k in range(1, top_count):
        combined = combined + gate_probs[:, k : k + 1] * outs[k]
    mixed = (inputs + combined).astype(jnp.bfloat16)
    grad_probs = jnp.stack([jnp.sum(grad_in * o, axis=1) for o in outs], axis=1)
    grad_normed = backs[0]
    for k in range(1, top_count):
        grad_normed = grad_normed + backs[k]
    grad_scaled = grad_normed * norm_gain
    grad_tokens = (
        grad_in
        + inverse_rms
        * (grad_scaled - normed * jnp.mean(grad_scaled * normed, axis=1, keepdims=True))
    ).astype(jnp.bfloat16)
    return (
        mixed,
        grad_probs,
        grad_gain,
        grad_tokens,
        grad_gate[None],
        grad_up[None],
        grad_down[None],
    )


def solution(mesh):
    rows = P(AXES, None)
    stacked = P(AXES, None, None)
    return jax.shard_map(
        on_device,
        mesh=mesh,
        in_specs=(rows, rows, rows, P(), stacked, stacked, stacked, rows),
        out_specs=(rows, rows, P(), rows, stacked, stacked, stacked),
        check_vma=False,
    )
```

```python
import jax
import jax.numpy as jnp
from jax import lax
from jax.sharding import PartitionSpec as P

AXES = ("expert", "dp")


def exchange(rows):
    return lax.all_to_all(rows, AXES, split_axis=0, concat_axis=0, tiled=True)


def contract(left, right, left_dim, right_dim):
    return lax.dot_general(
        left, right, (((left_dim,), (right_dim,)), ((), ())), preferred_element_type=jnp.float32
    )


def all_sum(part, devices_all, steps):
    total = part
    for step in steps:
        pairs = [(i, i ^ step) for i in range(devices_all)]
        total = total + lax.ppermute(total, AXES, pairs)
    return total


def expert_pass(arrived, arrived_grad, gate_matrix, up_matrix, down_matrix):
    pre_gate = jnp.dot(arrived, gate_matrix, preferred_element_type=jnp.float32)
    up_value = jnp.dot(arrived, up_matrix, preferred_element_type=jnp.float32)
    sigmoid_gate = jax.nn.sigmoid(pre_gate)
    activated = pre_gate * sigmoid_gate
    hidden = (activated * up_value).astype(jnp.bfloat16)
    expert_out = jnp.dot(hidden, down_matrix, preferred_element_type=jnp.float32).astype(
        jnp.bfloat16
    )
    grad_hidden = contract(arrived_grad, down_matrix, 1, 1)
    grad_down = contract(hidden, arrived_grad, 0, 0).astype(jnp.bfloat16)
    grad_pre = (
        grad_hidden * up_value * sigmoid_gate * (1.0 + pre_gate * (1.0 - sigmoid_gate))
    ).astype(jnp.bfloat16)
    grad_upval = (grad_hidden * activated).astype(jnp.bfloat16)
    grad_back = (
        contract(grad_pre, gate_matrix, 1, 1) + contract(grad_upval, up_matrix, 1, 1)
    ).astype(jnp.bfloat16)
    grad_gate = contract(arrived, grad_pre, 0, 0).astype(jnp.bfloat16)
    grad_up = contract(arrived, grad_upval, 0, 0).astype(jnp.bfloat16)
    return expert_out, grad_back, grad_gate, grad_up, grad_down


def on_device(tokens, routes, gate_probs, norm_gain, w_gate, w_up, w_down, out_grad):
    devices_all = lax.axis_size(AXES)
    tok_rows, width = tokens.shape
    top_count = routes.shape[1]
    assigned = tok_rows * top_count
    capacity = 2 * assigned // devices_all
    slots = devices_all * capacity
    inputs = tokens.astype(jnp.float32)
    inverse_rms = lax.rsqrt(jnp.mean(inputs * inputs, axis=1, keepdims=True) + 1e-06)
    normed = inputs * inverse_rms
    flat_ids = routes.reshape(assigned)
    onehot = (flat_ids[:, None] == jnp.arange(devices_all, dtype=jnp.int32)[None, :]).astype(
        jnp.int32
    )
    earlier = jnp.cumsum(onehot, axis=0) - onehot
    slot_index = flat_ids * capacity + jnp.sum(earlier * onehot, axis=1)
    select = (slot_index[:, None] == jnp.arange(slots, dtype=jnp.int32)[None, :]).astype(
        jnp.bfloat16
    )
    select_tk = select.reshape(tok_rows, top_count, slots)
    select_tok = jnp.sum(select_tk, axis=1)
    grad_in = out_grad.astype(jnp.float32)
    grad_rows = (gate_probs[:, :, None] * grad_in[:, None, :]).astype(jnp.bfloat16)
    sel_tok3 = select_tok.reshape(tok_rows, devices_all, capacity)
    sel_tk3 = select_tk.reshape(tok_rows, top_count, devices_all, capacity)
    send_scaled = lax.dot_general(sel_tok3, tokens, (((0,), (0,)), ((), ())), preferred_element_type=jnp.float32).astype(jnp.bfloat16)
    send_grad = lax.dot_general(
        sel_tk3, grad_rows, (((0, 1), (0, 1)), ((), ())), preferred_element_type=jnp.float32
    ).astype(jnp.bfloat16)
    sent = jnp.concatenate([send_scaled, send_grad], axis=2)
    arrived_all = exchange(sent).reshape(slots, 2 * width)
    arrived_inputs = arrived_all[:, :width].astype(jnp.float32)
    arrived_rms = lax.rsqrt(
        jnp.mean(arrived_inputs * arrived_inputs, axis=1, keepdims=True) + 1e-06
    )
    arrived_normed = arrived_inputs * arrived_rms
    arrived = (arrived_normed * norm_gain).astype(jnp.bfloat16)
    arrived_grad = arrived_all[:, width:]
    expert_out, grad_back, grad_gate, grad_up, grad_down = expert_pass(
        arrived, arrived_grad, w_gate[0], w_up[0], w_down[0]
    )
    gain_part = jnp.sum(grad_back.astype(jnp.float32) * arrived_normed, axis=0)
    back = jnp.concatenate([expert_out, grad_back], axis=1).reshape(
        devices_all, capacity, 2 * width
    )
    bits = [1 << b for b in (6, 5, 2, 0, 1, 3, 4)]
    gain_part = all_sum(gain_part, devices_all, bits[:3])
    back, gain_part = lax.optimization_barrier((back, gain_part))
    returned, grad_gate, grad_up, grad_down, gain_part = lax.optimization_barrier(
        (exchange(back), grad_gate, grad_up, grad_down, gain_part)
    )
    grad_gain = all_sum(gain_part, devices_all, bits[3:])
    returned = returned.reshape(slots, 2 * width)
    picked = [
        contract(select_tk[:, k, :], returned, 1, 0) for k in range(top_count)
    ]
    outs = [p[:, :width] for p in picked]
    backs = [p[:, width:] for p in picked]
    combined = gate_probs[:, 0:1] * outs[0]
    for k in range(1, top_count):
        combined = combined + gate_probs[:, k : k + 1] * outs[k]
    mixed = (inputs + combined).astype(jnp.bfloat16)
    grad_probs = jnp.stack([jnp.sum(grad_in * o, axis=1) for o in outs], axis=1)
    grad_normed = backs[0]
    for k in range(1, top_count):
        grad_normed = grad_normed + backs[k]
    grad_scaled = grad_normed * norm_gain
    grad_tokens = (
        grad_in
        + inverse_rms
        * (grad_scaled - normed * jnp.mean(grad_scaled * normed, axis=1, keepdims=True))
    ).astype(jnp.bfloat16)
    return (
        mixed,
        grad_probs,
        grad_gain,
        grad_tokens,
        grad_gate[None],
        grad_up[None],
        grad_down[None],
    )


def solution(mesh):
    rows = P(AXES, None)
    stacked = P(AXES, None, None)
    return jax.shard_map(
        on_device,
        mesh=mesh,
        in_specs=(rows, rows, rows, P(), stacked, stacked, stacked, rows),
        out_specs=(rows, rows, P(), rows, stacked, stacked, stacked),
        check_vma=False,
    )
```

```python
import jax
import jax.numpy as jnp
from jax import lax
from jax.sharding import PartitionSpec as P

AXES = ("expert", "dp")


def exchange(rows):
    return lax.all_to_all(rows, AXES, split_axis=0, concat_axis=0, tiled=True)


def contract(left, right, left_dim, right_dim):
    return lax.dot_general(
        left, right, (((left_dim,), (right_dim,)), ((), ())), preferred_element_type=jnp.float32
    )


def all_sum(part, devices_all, steps):
    total = part
    for step in steps:
        pairs = [(i, i ^ step) for i in range(devices_all)]
        total = total + lax.ppermute(total, AXES, pairs)
    return total


def expert_pass(arrived, arrived_grad, gate_matrix, up_matrix, down_matrix):
    pre_gate = jnp.dot(arrived, gate_matrix, preferred_element_type=jnp.float32)
    up_value = jnp.dot(arrived, up_matrix, preferred_element_type=jnp.float32)
    sigmoid_gate = jax.nn.sigmoid(pre_gate)
    activated = pre_gate * sigmoid_gate
    hidden = (activated * up_value).astype(jnp.bfloat16)
    expert_out = jnp.dot(hidden, down_matrix, preferred_element_type=jnp.float32).astype(
        jnp.bfloat16
    )
    grad_hidden = contract(arrived_grad, down_matrix, 1, 1)
    grad_down = contract(hidden, arrived_grad, 0, 0).astype(jnp.bfloat16)
    grad_pre = (
        grad_hidden * up_value * sigmoid_gate * (1.0 + pre_gate * (1.0 - sigmoid_gate))
    ).astype(jnp.bfloat16)
    grad_upval = (grad_hidden * activated).astype(jnp.bfloat16)
    grad_back = (
        contract(grad_pre, gate_matrix, 1, 1) + contract(grad_upval, up_matrix, 1, 1)
    ).astype(jnp.bfloat16)
    grad_gate = contract(arrived, grad_pre, 0, 0).astype(jnp.bfloat16)
    grad_up = contract(arrived, grad_upval, 0, 0).astype(jnp.bfloat16)
    return expert_out, grad_back, grad_gate, grad_up, grad_down


def on_device(tokens, routes, gate_probs, norm_gain, w_gate, w_up, w_down, out_grad):
    devices_all = lax.axis_size(AXES)
    tok_rows, width = tokens.shape
    top_count = routes.shape[1]
    assigned = tok_rows * top_count
    capacity = 2 * assigned // devices_all
    slots = devices_all * capacity
    flat_ids = routes.reshape(assigned)
    onehot = (flat_ids[:, None] == jnp.arange(devices_all, dtype=jnp.int32)[None, :]).astype(
        jnp.int32
    )
    earlier = jnp.cumsum(onehot, axis=0) - onehot
    slot_index = flat_ids * capacity + jnp.sum(earlier * onehot, axis=1)
    select = (slot_index[:, None] == jnp.arange(slots, dtype=jnp.int32)[None, :]).astype(
        jnp.bfloat16
    )
    select_tk = select.reshape(tok_rows, top_count, slots)
    select_tok = jnp.sum(select_tk, axis=1)
    grad_rows = (gate_probs[:, :, None] * out_grad.astype(jnp.float32)[:, None, :]).astype(
        jnp.bfloat16
    )
    sel_tok3 = select_tok.reshape(tok_rows, devices_all, capacity)
    sel_tk3 = select_tk.reshape(tok_rows, top_count, devices_all, capacity)
    send_scaled = lax.dot_general(sel_tok3, tokens, (((0,), (0,)), ((), ())), preferred_element_type=jnp.float32).astype(jnp.bfloat16)
    send_grad = lax.dot_general(
        sel_tk3, grad_rows, (((0, 1), (0, 1)), ((), ())), preferred_element_type=jnp.float32
    ).astype(jnp.bfloat16)
    sent = jnp.concatenate([send_scaled, send_grad], axis=2)
    arrived_all = exchange(sent).reshape(slots, 2 * width)
    arrived_inputs = arrived_all[:, :width].astype(jnp.float32)
    arrived_rms = lax.rsqrt(
        jnp.mean(arrived_inputs * arrived_inputs, axis=1, keepdims=True) + 1e-06
    )
    arrived_normed = arrived_inputs * arrived_rms
    arrived = (arrived_normed * norm_gain).astype(jnp.bfloat16)
    arrived_grad = arrived_all[:, width:]
    expert_out, grad_back, grad_gate, grad_up, grad_down = expert_pass(
        arrived, arrived_grad, w_gate[0], w_up[0], w_down[0]
    )
    gain_part = jnp.sum(grad_back.astype(jnp.float32) * arrived_normed, axis=0)
    back = jnp.concatenate([expert_out, grad_back], axis=1).reshape(
        devices_all, capacity, 2 * width
    )
    bits = [1 << b for b in range(devices_all.bit_length() - 1)]
    gain_part = all_sum(gain_part, devices_all, bits[:3])
    back, gain_part = lax.optimization_barrier((back, gain_part))
    returned, grad_gate, grad_up, grad_down, gain_part, late_grad, late_tokens = (
        lax.optimization_barrier(
            (exchange(back), grad_gate, grad_up, grad_down, gain_part, out_grad, tokens)
        )
    )
    inputs = late_tokens.astype(jnp.float32)
    inverse_rms = lax.rsqrt(jnp.mean(inputs * inputs, axis=1, keepdims=True) + 1e-06)
    normed = inputs * inverse_rms
    grad_in = late_grad.astype(jnp.float32)
    grad_gain = all_sum(gain_part, devices_all, bits[3:])
    returned = returned.reshape(slots, 2 * width)
    picked = [
        contract(select_tk[:, k, :], returned, 1, 0) for k in range(top_count)
    ]
    outs = [p[:, :width] for p in picked]
    backs = [p[:, width:] for p in picked]
    combined = gate_probs[:, 0:1] * outs[0]
    for k in range(1, top_count):
        combined = combined + gate_probs[:, k : k + 1] * outs[k]
    mixed = (inputs + combined).astype(jnp.bfloat16)
    grad_probs = jnp.stack([jnp.sum(grad_in * o, axis=1) for o in outs], axis=1)
    grad_normed = backs[0]
    for k in range(1, top_count):
        grad_normed = grad_normed + backs[k]
    grad_scaled = grad_normed * norm_gain
    grad_tokens = (
        grad_in
        + inverse_rms
        * (grad_scaled - normed * jnp.mean(grad_scaled * normed, axis=1, keepdims=True))
    ).astype(jnp.bfloat16)
    return (
        mixed,
        grad_probs,
        grad_gain,
        grad_tokens,
        grad_gate[None],
        grad_up[None],
        grad_down[None],
    )


def solution(mesh):
    rows = P(AXES, None)
    stacked = P(AXES, None, None)
    return jax.shard_map(
        on_device,
        mesh=mesh,
        in_specs=(rows, rows, rows, P(), stacked, stacked, stacked, rows),
        out_specs=(rows, rows, P(), rows, stacked, stacked, stacked),
        check_vma=False,
    )
```
